128 devices in a mesh: row: 8 (over x_hi, z), col: 16 (over x_lo, y, core).
Axes of the slice: x: 4 (x_hi: 2, x_lo: 2; x = x_hi * 2 + x_lo), y: 4, z: 4, core: 2. Of those that a mesh axis runs over, the one named last changes fastest.
Arguments:
- leaf_inverse: bfloat16 [2048, 256, 256], P(('row', 'col')), may hold values from -0.375 to 0.375
- leaf_coupling: bfloat16 [2048, 256, 256], P(('row', 'col')), may hold values from -0.375 to 0.375
- window_coupling: bfloat16 [2048, 256, 1024], P(('row', 'col')), may hold values from -6 to 6
- leaf_rows: int32 [2048, 256], P(('row', 'col')), may hold values from 0 to 2047
- leaf_sizes: int32 [2048], P(('row', 'col')), may hold values from 128 to 256
- owner_table: int32 [8, 32], P('row'), may hold values from 0 to 31, each once within a row
- schur_block: float32 [16384, 1024], P(('row', 'col')), may hold values from 0 to 1006
- prior_panels: float32 [16384, 1024], P(('row', 'col')), may hold values from -1 to 1
Outputs:
- result_panel: float32 [16384, 1024], P(('row', 'col'))
The draws below stay inside these ranges and needn't reach their ends.
All inputs are finite; a program needn't handle non-finite values.
Results may differ from the reference program's by a relative error of at most 0.0003.
Values sent between devices are 32-bit elements; how exact they have to be, the bound alone decides.
No kernel may reach another device: no remote copies, remote signals or barrier semaphores. Data moves between devices by JAX's collectives and lax.ppermute only.
A program may use at most 128 MiB of HBM per device.

```python
import math
import jax
import jax.numpy as jnp
import numpy as np
from jax import lax

WIN = 1024
NB = 512
LS = 256
NI = 256
RB = 64
LPD = 16
RPD = 128
LEAVES = 2048
M = 16384
GROUP_ROWS = 2048
GB = 32
WPD = 8
N_ROW = 8
N_COL = 16


def draw_schur_block(key, part):
    base = 3.0 + jnp.clip(jax.random.normal(key, (M, WIN), jnp.float32), -3.0, 3.0)
    rows = jnp.arange(M, dtype=jnp.int32)[:, None]
    columns = jnp.arange(WIN, dtype=jnp.int32)[None, :]
    local_rows = rows % RPD
    on_diagonal = (local_rows < WPD) & (rows // RPD * WPD + local_rows == columns)
    return jnp.where(on_diagonal, base + 1000.0, base)


def draw_prior_panels(key, part):
    values = jnp.clip(0.2 * jax.random.normal(key, (M, 2 * NB), jnp.float32), -1.0, 1.0)
    return values


def draw_window_coupling(key, part):
    values = jnp.clip(jax.random.normal(key, (LEAVES, LS, WIN), jnp.float32), -6.0, 6.0)
    return values.astype(jnp.bfloat16)


def touch_ends(entries, key, smallest, high):
    dims = entries.shape
    spot = [jax.random.randint(jax.random.fold_in(key, axis), (), 0, dims[axis]) for axis in range(len(dims))]
    entries = entries.at[tuple(spot)].set(smallest)
    longest = dims.index(max(dims))
    spot[longest] = (spot[longest] + 1) % dims[longest]
    return entries.at[tuple(spot)].set(high)


def level_of(rng, shape, split, low, high):
    factor_of = 1.0
    for axis_at, shards_of in split:
        steps = jax.random.uniform(jax.random.fold_in(jax.random.fold_in(rng, 6), axis_at), (shards_of,), jnp.float32, low / len(split), high / len(split))
        factor_of = factor_of * jnp.repeat(jnp.exp(steps), shape[axis_at] // shards_of).reshape((-1,) + (1,) * (len(shape) - 1 - axis_at))
    return factor_of


def rank_table(count, slope):
    weights = [(1 << 20) // math.isqrt(standing ** slope) + 1 for standing in range(1, count + 1)]
    scale = 1 + sum(weights) // (1 << 30)
    return np.cumsum(np.array([max(1, weight // scale) for weight in weights]))


def ranked(rng, extent, amount, lean):
    grid = rank_table(amount, lean)
    pick = jax.random.randint(jax.random.fold_in(rng, 1), extent, 0, int(grid[amount - 1]))
    rank = jnp.searchsorted(jnp.asarray(grid, jnp.int32), pick, side="right")
    return jax.random.permutation(jax.random.fold_in(rng, 2), amount)[rank].astype(jnp.int32)


def scatter_about(rng, dims, scale, bound, cuts=(), kind=jnp.bfloat16):
    level = level_of(rng, dims, cuts, -0.22, 0.18) if cuts else 1.0
    array = jax.random.normal(rng, dims, jnp.float32) * scale * level
    return jnp.minimum(jnp.maximum(array, -bound), bound).astype(kind)


def setup_inputs(seed: int = 0) -> dict:
    splits = jax.random.split(jax.random.key(seed), 9)
    leaf_inverse = scatter_about(splits[0], (LEAVES, LS, LS), LS ** -0.5, 0.375, ((0, 128),))
    leaf_coupling = scatter_about(splits[1], (LEAVES, LS, NI), LS ** -0.5, 0.375, ((0, 128),))
    window_coupling = draw_window_coupling(jax.random.fold_in(splits[8], 71), 0)
    leaf_rows = touch_ends(ranked(splits[3], (LEAVES, NI), GROUP_ROWS, 1), jax.random.fold_in(splits[3], 3), 0, GROUP_ROWS - 1).astype(jnp.int32)
    leaf_sizes = touch_ends(jax.random.randint(splits[4], (LEAVES,), LS // 2, LS + 1), jax.random.fold_in(splits[4], 1), LS // 2, LS).astype(jnp.int32)
    owner_table = jax.vmap(lambda own: jax.random.permutation(own, GB))(jax.random.split(splits[5], N_ROW)).reshape((N_ROW, GB)).astype(jnp.int32)
    schur_block = draw_schur_block(jax.random.fold_in(splits[8], 71), 0)
    prior_panels = draw_prior_panels(jax.random.fold_in(splits[8], 71), 0)
    return dict(leaf_inverse=leaf_inverse, leaf_coupling=leaf_coupling, window_coupling=window_coupling, leaf_rows=leaf_rows, leaf_sizes=leaf_sizes, owner_table=owner_table, schur_block=schur_block, prior_panels=prior_panels)


def leaf_sum(inverse, coupling, window_part, rows, sizes, group_rows):
    position = jnp.arange(inverse.shape[1], dtype=jnp.int32)
    active = position[None, :, None] < sizes[:, None, None]
    masked = jnp.where(active, window_part, jnp.zeros_like(window_part)).astype(jnp.float32)
    solved = jnp.einsum('lij,ljw->liw', inverse.astype(jnp.float32), masked, precision=lax.Precision.HIGHEST)
    solved = jnp.where(active, solved, jnp.zeros_like(solved)).astype(jnp.bfloat16)
    solved = lax.optimization_barrier(solved).astype(jnp.float32)
    leaf_terms = jnp.einsum('lin,liw->lnw', coupling.astype(jnp.float32), solved, precision=lax.Precision.HIGHEST)
    width = window_part.shape[2]
    summed = jnp.zeros((group_rows, width), jnp.float32)
    return summed.at[rows.reshape(-1)].add(leaf_terms.reshape(-1, width))

def blocked_factor(block, panel_width):
    symmetric = 0.5 * (block + block.T)
    panel_count = symmetric.shape[0] // panel_width
    factor = jnp.zeros_like(symmetric)
    trailing = symmetric
    for step_index in range(panel_count):
        leading = jnp.linalg.cholesky(trailing[:panel_width, :panel_width])
        beneath = jax.scipy.linalg.solve_triangular(leading, trailing[panel_width:, :panel_width].T, lower=True).T
        offset = step_index * panel_width
        factor = factor.at[offset:offset + panel_width, offset:offset + panel_width].set(leading)
        factor = factor.at[offset + panel_width:, offset:offset + panel_width].set(beneath)
        trailing = trailing[panel_width:, panel_width:] - jnp.dot(beneath, beneath.T, precision=lax.Precision.HIGHEST)
    return factor

def reference(leaf_inverse, leaf_coupling, window_coupling, leaf_rows, leaf_sizes, owner_table, schur_block, prior_panels):
    per_group = N_COL * LPD
    group_rows = N_COL * RPD
    pieces = []
    for group in range(N_ROW):
        first = group * per_group
        summed = leaf_sum(leaf_inverse[first:first + per_group], leaf_coupling[first:first + per_group], window_coupling[first:first + per_group], leaf_rows[first:first + per_group], leaf_sizes[first:first + per_group], group_rows)
        blocks = summed.reshape(-1, RB, WIN)
        placed = jnp.zeros_like(blocks).at[owner_table[group]].set(blocks)
        pieces.append(placed.reshape(group_rows, WIN))
    reduced = jnp.concatenate(pieces, 0)
    coupled = schur_block - reduced
    devices_all = N_ROW * N_COL
    panels_win = prior_panels.reshape(devices_all, RPD, 2 * NB)[:, :WPD].reshape(WIN, 2 * NB)
    updated = coupled - jnp.dot(prior_panels, panels_win.T, precision=lax.Precision.HIGHEST)
    window_block = updated.reshape(devices_all, RPD, WIN)[:, :WPD].reshape(WIN, WIN)
    factor = blocked_factor(window_block, NB)
    return jax.scipy.linalg.solve_triangular(factor, updated.T, lower=True).T
```

```python
import jax
import jax.numpy as jnp
from jax import lax
from jax.sharding import PartitionSpec as P

NB = 512
RB = 64


def blocked_factor(block, panel_width):
    symmetric = 0.5 * (block + block.T)
    panel_count = symmetric.shape[0] // panel_width
    factor = jnp.zeros_like(symmetric)
    trailing = symmetric
    for step_index in range(panel_count):
        leading = jnp.linalg.cholesky(trailing[:panel_width, :panel_width])
        beneath = jax.scipy.linalg.solve_triangular(
            leading, trailing[panel_width:, :panel_width].T, lower=True
        ).T
        offset = step_index * panel_width
        factor = factor.at[offset : offset + panel_width, offset : offset + panel_width].set(
            leading
        )
        factor = factor.at[offset + panel_width :, offset : offset + panel_width].set(beneath)
        trailing = trailing[panel_width:, panel_width:] - jnp.dot(
            beneath, beneath.T, precision=lax.Precision.HIGHEST
        )
    return factor


def gather_rows(rows):
    within = lax.all_gather(rows, "col", axis=0, tiled=True)
    return lax.all_gather(within, "row", axis=0, tiled=True)


def body(
    leaf_inverse,
    leaf_coupling,
    window_coupling,
    leaf_rows,
    leaf_sizes,
    owner_table,
    schur_block,
    prior_panels,
):
    leaf_order = leaf_inverse.shape[1]
    col_width = window_coupling.shape[2]
    local_rows = schur_block.shape[0]
    group_rows = lax.axis_size("col") * local_rows
    window_rows = col_width // (lax.axis_size("row") * lax.axis_size("col"))
    position = jnp.arange(leaf_order, dtype=jnp.int32)
    active = position[None, :, None] < leaf_sizes[:, None, None]
    masked = jnp.where(active, window_coupling, jnp.zeros_like(window_coupling))
    solved = jnp.einsum("lij,ljw->liw", leaf_inverse, masked, preferred_element_type=jnp.float32)
    solved = jnp.where(active, solved, jnp.zeros_like(solved)).astype(jnp.bfloat16)
    leaf_terms = jnp.einsum(
        "lin,liw->lnw", leaf_coupling, solved, preferred_element_type=jnp.float32
    )
    summed = jnp.zeros((group_rows, col_width), jnp.float32)
    summed = summed.at[leaf_rows.reshape(-1)].add(leaf_terms.reshape(-1, col_width))
    blocks = summed.reshape(-1, RB, col_width)
    placed = jnp.zeros_like(blocks).at[owner_table[0]].set(blocks).reshape(group_rows, col_width)
    reduced = lax.psum_scatter(placed, "col", scatter_dimension=0, tiled=True)
    coupled = schur_block - reduced
    panels_win = gather_rows(prior_panels[:window_rows])
    updated = coupled - jnp.dot(prior_panels, panels_win.T, precision=lax.Precision.HIGHEST)
    window_block = gather_rows(updated[:window_rows])
    factor = blocked_factor(window_block, NB)
    return jax.scipy.linalg.solve_triangular(factor, updated.T, lower=True).T


def solution(mesh):
    placed = (
        P(("row", "col"), None, None),
        P(("row", "col"), None, None),
        P(("row", "col"), None, None),
        P(("row", "col"), None),
        P(("row", "col")),
        P("row", None),
        P(("row", "col"), None),
        P(("row", "col"), None),
    )
    return jax.shard_map(
        body, mesh=mesh, in_specs=placed, out_specs=P(("row", "col"), None), check_vma=False
    )
```

```python
import jax
import jax.numpy as jnp
from jax import lax
from jax.experimental import pallas as pl
from jax.experimental.pallas import tpu as pltpu
from jax.sharding import PartitionSpec as P

RB = 64
BS = 128
HI = lax.Precision.HIGHEST


def _nt(a, b):
    return lax.dot_general(a, b, (((1,), (1,)), ((), ())), precision=HI,
                           preferred_element_type=jnp.float32)


def _nn(a, b):
    return lax.dot_general(a, b, (((1,), (0,)), ((), ())), precision=HI,
                           preferred_element_type=jnp.float32)


def _block_inverse(blk_ref, inv_ref):
    lane = lax.broadcasted_iota(jnp.int32, (1, BS), 1)
    sub = lax.broadcasted_iota(jnp.int32, (BS, BS), 0)
    inv_ref[...] = jnp.where(sub == lax.broadcasted_iota(jnp.int32, (BS, BS), 1), 1.0, 0.0).astype(jnp.float32)

    def step(j, carry):
        r = blk_ref[pl.ds(j, 1), :]
        d = jnp.sum(jnp.where(lane == j, r, 0.0), axis=1, keepdims=True)
        scale = 1.0 / jnp.sqrt(d)
        c = jnp.where(lane >= j, r * scale, 0.0)
        a = blk_ref[...]
        col = jnp.sum(jnp.where(lax.broadcasted_iota(jnp.int32, (BS, BS), 1) == j, a, 0.0), axis=1, keepdims=True) * scale
        col = jnp.where(lax.broadcasted_iota(jnp.int32, (BS, 1), 0) >= j, col, 0.0)
        blk_ref[...] = a - col * c
        m_row = inv_ref[pl.ds(j, 1), :] * scale
        below = jnp.where(lax.broadcasted_iota(jnp.int32, (BS, 1), 0) > j, col, 0.0)
        inv_ref[...] = inv_ref[...] - below * m_row
        inv_ref[pl.ds(j, 1), :] = m_row
        return carry

    lax.fori_loop(0, BS, step, 0)


def _kernel(s_ref, u_ref, o_ref, a_ref, l_ref, m_ref, blk_ref, inv_ref):
    n = s_ref.shape[0]
    nb = n // BS
    a_ref[...] = s_ref[...]
    for k in range(nb):
        lo = k * BS
        blk_ref[...] = a_ref[lo:lo + BS, lo:lo + BS]
        _block_inverse(blk_ref, inv_ref)
        mkk = inv_ref[...]
        m_ref[k] = mkk
        if k + 1 < nb:
            panel = _nt(a_ref[lo + BS:, lo:lo + BS], mkk)
            l_ref[lo + BS:, lo:lo + BS] = panel
            a_ref[lo + BS:, lo + BS:] = a_ref[lo + BS:, lo + BS:] - _nt(panel, panel)
    for j in range(nb):
        lo = j * BS
        acc = u_ref[:, lo:lo + BS]
        if j > 0:
            acc = acc - _nt(o_ref[:, :lo], l_ref[lo:lo + BS, :lo])
        o_ref[:, lo:lo + BS] = _nt(acc, m_ref[j])


def factor_solve(symmetric, rows):
    n = symmetric.shape[0]
    m = rows.shape[0]
    return pl.pallas_call(
        _kernel,
        out_shape=jax.ShapeDtypeStruct((m, n), jnp.float32),
        scratch_shapes=[
            pltpu.VMEM((n, n), jnp.float32),
            pltpu.VMEM((n, n), jnp.float32),
            pltpu.VMEM((n // BS, BS, BS), jnp.float32),
            pltpu.VMEM((BS, BS), jnp.float32),
            pltpu.VMEM((BS, BS), jnp.float32),
        ],
        compiler_params=pltpu.CompilerParams(vmem_limit_bytes=60 * 1024 * 1024),
    )(symmetric, rows)


def gather_rows(rows):
    within = lax.all_gather(rows, "col", axis=0, tiled=True)
    return lax.all_gather(within, "row", axis=0, tiled=True)


def body(
    leaf_inverse,
    leaf_coupling,
    window_coupling,
    leaf_rows,
    leaf_sizes,
    owner_table,
    schur_block,
    prior_panels,
):
    leaf_order = leaf_inverse.shape[1]
    col_width = window_coupling.shape[2]
    local_rows = schur_block.shape[0]
    group_rows = lax.axis_size("col") * local_rows
    window_rows = col_width // (lax.axis_size("row") * lax.axis_size("col"))
    position = jnp.arange(leaf_order, dtype=jnp.int32)
    active = position[None, :, None] < leaf_sizes[:, None, None]
    masked = jnp.where(active, window_coupling, jnp.zeros_like(window_coupling))
    solved = jnp.einsum("lij,ljw->liw", leaf_inverse, masked, preferred_element_type=jnp.float32)
    solved = jnp.where(active, solved, jnp.zeros_like(solved)).astype(jnp.bfloat16)
    leaf_terms = jnp.einsum(
        "lin,liw->lnw", leaf_coupling, solved, preferred_element_type=jnp.float32
    )
    summed = jnp.zeros((group_rows, col_width), jnp.float32)
    summed = summed.at[leaf_rows.reshape(-1)].add(leaf_terms.reshape(-1, col_width))
    blocks = summed.reshape(-1, RB, col_width)
    placed = jnp.zeros_like(blocks).at[owner_table[0]].set(blocks).reshape(group_rows, col_width)
    reduced = lax.psum_scatter(placed, "col", scatter_dimension=0, tiled=True)
    coupled = schur_block - reduced
    panels_win = gather_rows(prior_panels[:window_rows])
    updated = coupled - jnp.dot(prior_panels, panels_win.T, precision=lax.Precision.HIGHEST)
    window_block = gather_rows(updated[:window_rows])
    symmetric = 0.5 * (window_block + window_block.T)
    return factor_solve(symmetric, updated)


def solution(mesh):
    placed = (
        P(("row", "col"), None, None),
        P(("row", "col"), None, None),
        P(("row", "col"), None, None),
        P(("row", "col"), None),
        P(("row", "col")),
        P("row", None),
        P(("row", "col"), None),
        P(("row", "col"), None),
    )
    return jax.shard_map(
        body, mesh=mesh, in_specs=placed, out_specs=P(("row", "col"), None), check_vma=False
    )
```

```python
import jax
import jax.numpy as jnp
from jax import lax
from jax.experimental import pallas as pl
from jax.experimental.pallas import tpu as pltpu
from jax.sharding import PartitionSpec as P

RB = 64
BS = 128
HI = lax.Precision.HIGHEST


def _nt(a, b):
    return lax.dot_general(a, b, (((1,), (1,)), ((), ())), precision=HI,
                           preferred_element_type=jnp.float32)


def _nn(a, b):
    return lax.dot_general(a, b, (((1,), (0,)), ((), ())), precision=HI,
                           preferred_element_type=jnp.float32)


def _block_inverse(blk_ref, inv_ref):
    lane = lax.broadcasted_iota(jnp.int32, (1, BS), 1)
    sub = lax.broadcasted_iota(jnp.int32, (BS, BS), 0)
    inv_ref[...] = jnp.where(sub == lax.broadcasted_iota(jnp.int32, (BS, BS), 1), 1.0, 0.0).astype(jnp.float32)

    def step(j, carry):
        r = blk_ref[pl.ds(j, 1), :]
        d = jnp.sum(jnp.where(lane == j, r, 0.0), axis=1, keepdims=True)
        scale = 1.0 / jnp.sqrt(d)
        c = jnp.where(lane >= j, r * scale, 0.0)
        a = blk_ref[...]
        col = jnp.sum(jnp.where(lax.broadcasted_iota(jnp.int32, (BS, BS), 1) == j, a, 0.0), axis=1, keepdims=True) * scale
        col = jnp.where(lax.broadcasted_iota(jnp.int32, (BS, 1), 0) >= j, col, 0.0)
        blk_ref[...] = a - col * c
        m_row = inv_ref[pl.ds(j, 1), :] * scale
        below = jnp.where(lax.broadcasted_iota(jnp.int32, (BS, 1), 0) > j, col, 0.0)
        inv_ref[...] = inv_ref[...] - below * m_row
        inv_ref[pl.ds(j, 1), :] = m_row
        return carry

    lax.fori_loop(0, BS, step, 0)


def _kernel(s_ref, u_ref, o_ref, a_ref, l_ref, m_ref, blk_ref, inv_ref):
    n = s_ref.shape[0]
    nb = n // BS
    a_ref[...] = s_ref[...]
    for k in range(nb):
        lo = k * BS
        blk_ref[...] = a_ref[lo:lo + BS, lo:lo + BS]
        _block_inverse(blk_ref, inv_ref)
        mkk = inv_ref[...]
        m_ref[k] = mkk
        if k + 1 < nb:
            panel = _nt(a_ref[lo + BS:, lo:lo + BS], mkk)
            l_ref[lo + BS:, lo:lo + BS] = panel
            a_ref[lo + BS:, lo + BS:] = a_ref[lo + BS:, lo + BS:] - _nt(panel, panel)
    for j in range(nb):
        lo = j * BS
        acc = u_ref[:, lo:lo + BS]
        if j > 0:
            acc = acc - _nt(o_ref[:, :lo], l_ref[lo:lo + BS, :lo])
        o_ref[:, lo:lo + BS] = _nt(acc, m_ref[j])


def factor_solve(symmetric, rows):
    n = symmetric.shape[0]
    m = rows.shape[0]
    return pl.pallas_call(
        _kernel,
        out_shape=jax.ShapeDtypeStruct((m, n), jnp.float32),
        scratch_shapes=[
            pltpu.VMEM((n, n), jnp.float32),
            pltpu.VMEM((n, n), jnp.float32),
            pltpu.VMEM((n // BS, BS, BS), jnp.float32),
            pltpu.VMEM((BS, BS), jnp.float32),
            pltpu.VMEM((BS, BS), jnp.float32),
        ],
        compiler_params=pltpu.CompilerParams(vmem_limit_bytes=60 * 1024 * 1024),
    )(symmetric, rows)


def gather_rows(rows):
    n_row = lax.axis_size("row")
    n_col = lax.axis_size("col")
    across = lax.all_gather(rows, "row", axis=0, tiled=True)
    both = lax.all_gather(across, "col", axis=0, tiled=True)
    both = both.reshape(n_col, n_row, rows.shape[0], rows.shape[1])
    return both.transpose(1, 0, 2, 3).reshape(-1, rows.shape[1])


def body(
    leaf_inverse,
    leaf_coupling,
    window_coupling,
    leaf_rows,
    leaf_sizes,
    owner_table,
    schur_block,
    prior_panels,
):
    leaf_order = leaf_inverse.shape[1]
    col_width = window_coupling.shape[2]
    local_rows = schur_block.shape[0]
    group_rows = lax.axis_size("col") * local_rows
    window_rows = col_width // (lax.axis_size("row") * lax.axis_size("col"))
    position = jnp.arange(leaf_order, dtype=jnp.int32)
    active = position[None, :, None] < leaf_sizes[:, None, None]
    masked = jnp.where(active, window_coupling, jnp.zeros_like(window_coupling))
    solved = jnp.einsum("lij,ljw->liw", leaf_inverse, masked, preferred_element_type=jnp.float32)
    solved = jnp.where(active, solved, jnp.zeros_like(solved)).astype(jnp.bfloat16)
    leaf_terms = jnp.einsum(
        "lin,liw->lnw", leaf_coupling, solved, preferred_element_type=jnp.float32
    )
    targets = owner_table[0][leaf_rows // RB] * RB + leaf_rows % RB
    placed = jnp.zeros((group_rows, col_width), jnp.float32)
    placed = placed.at[targets.reshape(-1)].add(leaf_terms.reshape(-1, col_width))
    reduced = lax.psum_scatter(placed, "col", scatter_dimension=0, tiled=True)
    coupled = schur_block - reduced
    panels_win = gather_rows(prior_panels[:window_rows])
    updated = coupled - jnp.dot(prior_panels, panels_win.T, precision=lax.Precision.HIGHEST)
    window_block = gather_rows(updated[:window_rows])
    symmetric = 0.5 * (window_block + window_block.T)
    return factor_solve(symmetric, updated)


def solution(mesh):
    placed = (
        P(("row", "col"), None, None),
        P(("row", "col"), None, None),
        P(("row", "col"), None, None),
        P(("row", "col"), None),
        P(("row", "col")),
        P("row", None),
        P(("row", "col"), None),
        P(("row", "col"), None),
    )
    return jax.shard_map(
        body, mesh=mesh, in_specs=placed, out_specs=P(("row", "col"), None), check_vma=False
    )
```

```python
import jax
import jax.numpy as jnp
from jax import lax
from jax.experimental import pallas as pl
from jax.experimental.pallas import tpu as pltpu
from jax.sharding import PartitionSpec as P

RB = 64
BS = 128
HI = lax.Precision.HIGHEST


def _nt(a, b):
    return lax.dot_general(a, b, (((1,), (1,)), ((), ())), precision=HI,
                           preferred_element_type=jnp.float32)


def _nn(a, b):
    return lax.dot_general(a, b, (((1,), (0,)), ((), ())), precision=HI,
                           preferred_element_type=jnp.float32)


def _block_inverse(blk_ref, inv_ref):
    lane = lax.broadcasted_iota(jnp.int32, (1, BS), 1)
    sub = lax.broadcasted_iota(jnp.int32, (BS, BS), 0)
    inv_ref[...] = jnp.where(sub == lax.broadcasted_iota(jnp.int32, (BS, BS), 1), 1.0, 0.0).astype(jnp.float32)

    def step(j, carry):
        r = blk_ref[pl.ds(j, 1), :]
        d = jnp.sum(jnp.where(lane == j, r, 0.0), axis=1, keepdims=True)
        scale = 1.0 / jnp.sqrt(d)
        c = jnp.where(lane >= j, r * scale, 0.0)
        a = blk_ref[...]
        col = jnp.sum(jnp.where(lax.broadcasted_iota(jnp.int32, (BS, BS), 1) == j, a, 0.0), axis=1, keepdims=True) * scale
        col = jnp.where(lax.broadcasted_iota(jnp.int32, (BS, 1), 0) >= j, col, 0.0)
        blk_ref[...] = a - col * c
        m_row = inv_ref[pl.ds(j, 1), :] * scale
        below = jnp.where(lax.broadcasted_iota(jnp.int32, (BS, 1), 0) > j, col, 0.0)
        inv_ref[...] = inv_ref[...] - below * m_row
        inv_ref[pl.ds(j, 1), :] = m_row
        return carry

    lax.fori_loop(0, BS, step, 0)


def _kernel(s_ref, u_ref, o_ref, a_ref, l_ref, m_ref, blk_ref, inv_ref):
    n = s_ref.shape[0]
    nb = n // BS
    a_ref[...] = s_ref[...]
    for k in range(nb):
        lo = k * BS
        blk_ref[...] = a_ref[lo:lo + BS, lo:lo + BS]
        _block_inverse(blk_ref, inv_ref)
        mkk = inv_ref[...]
        m_ref[k] = mkk
        if k + 1 < nb:
            panel = _nt(a_ref[lo + BS:, lo:lo + BS], mkk)
            l_ref[lo + BS:, lo:lo + BS] = panel
            a_ref[lo + BS:, lo + BS:] = a_ref[lo + BS:, lo + BS:] - _nt(panel, panel)
    for j in range(nb):
        lo = j * BS
        acc = u_ref[:, lo:lo + BS]
        if j > 0:
            acc = acc - _nt(o_ref[:, :lo], l_ref[lo:lo + BS, :lo])
        o_ref[:, lo:lo + BS] = _nt(acc, m_ref[j])


def factor_solve(symmetric, rows):
    n = symmetric.shape[0]
    m = rows.shape[0]
    return pl.pallas_call(
        _kernel,
        out_shape=jax.ShapeDtypeStruct((m, n), jnp.float32),
        scratch_shapes=[
            pltpu.VMEM((n, n), jnp.float32),
            pltpu.VMEM((n, n), jnp.float32),
            pltpu.VMEM((n // BS, BS, BS), jnp.float32),
            pltpu.VMEM((BS, BS), jnp.float32),
            pltpu.VMEM((BS, BS), jnp.float32),
        ],
        compiler_params=pltpu.CompilerParams(vmem_limit_bytes=60 * 1024 * 1024),
    )(symmetric, rows)


def gather_rows_col_first(rows):
    within = lax.all_gather(rows, "col", axis=0, tiled=True)
    return lax.all_gather(within, "row", axis=0, tiled=True)


def gather_rows(rows):
    n_row = lax.axis_size("row")
    n_col = lax.axis_size("col")
    across = lax.all_gather(rows, "row", axis=0, tiled=True)
    both = lax.all_gather(across, "col", axis=0, tiled=True)
    both = both.reshape(n_col, n_row, rows.shape[0], rows.shape[1])
    return both.transpose(1, 0, 2, 3).reshape(-1, rows.shape[1])


def body(
    leaf_inverse,
    leaf_coupling,
    window_coupling,
    leaf_rows,
    leaf_sizes,
    owner_table,
    schur_block,
    prior_panels,
):
    leaf_order = leaf_inverse.shape[1]
    col_width = window_coupling.shape[2]
    local_rows = schur_block.shape[0]
    group_rows = lax.axis_size("col") * local_rows
    window_rows = col_width // (lax.axis_size("row") * lax.axis_size("col"))
    position = jnp.arange(leaf_order, dtype=jnp.int32)
    active = position[None, :, None] < leaf_sizes[:, None, None]
    masked = jnp.where(active, window_coupling, jnp.zeros_like(window_coupling))
    solved = jnp.einsum("lij,ljw->liw", leaf_inverse, masked, preferred_element_type=jnp.float32)
    solved = jnp.where(active, solved, jnp.zeros_like(solved)).astype(jnp.bfloat16)
    leaf_terms = jnp.einsum(
        "lin,liw->lnw", leaf_coupling, solved, preferred_element_type=jnp.float32
    )
    block_of = leaf_rows // RB
    slots = lax.broadcasted_iota(jnp.int32, (1, 1, owner_table.shape[1]), 2)
    shift = jnp.sum(
        jnp.where(block_of[:, :, None] == slots, owner_table[0][None, None, :] - slots, 0), axis=2
    )
    targets = leaf_rows + shift * RB
    placed = jnp.zeros((group_rows, col_width), jnp.float32)
    placed = placed.at[targets.reshape(-1)].add(leaf_terms.reshape(-1, col_width))
    reduced = lax.psum_scatter(placed, "col", scatter_dimension=0, tiled=True)
    panels_win = gather_rows_col_first(prior_panels[:window_rows])
    partial = schur_block - jnp.dot(prior_panels, panels_win.T, precision=lax.Precision.HIGHEST)
    partial = lax.optimization_barrier(partial)
    updated = partial - reduced
    window_block = gather_rows(updated[:window_rows])
    symmetric = 0.5 * (window_block + window_block.T)
    return factor_solve(symmetric, updated)


def solution(mesh):
    placed = (
        P(("row", "col"), None, None),
        P(("row", "col"), None, None),
        P(("row", "col"), None, None),
        P(("row", "col"), None),
        P(("row", "col")),
        P("row", None),
        P(("row", "col"), None),
        P(("row", "col"), None),
    )
    return jax.shard_map(
        body, mesh=mesh, in_specs=placed, out_specs=P(("row", "col"), None), check_vma=False
    )
```

```python
import jax
import jax.numpy as jnp
from jax import lax
from jax.experimental import pallas as pl
from jax.experimental.pallas import tpu as pltpu
from jax.sharding import PartitionSpec as P

RB = 64
BS = 128
MP = 64
HI = lax.Precision.HIGHEST


def _nt(a, b):
    return lax.dot_general(a, b, (((1,), (1,)), ((), ())), precision=HI,
                           preferred_element_type=jnp.float32)


def _tn(a, b):
    return lax.dot_general(a, b, (((0,), (0,)), ((), ())), precision=HI,
                           preferred_element_type=jnp.float32)


def _block_inverse(blk_ref, inv_ref):
    eye = lax.broadcasted_iota(jnp.int32, (BS, BS), 0) == lax.broadcasted_iota(jnp.int32, (BS, BS), 1)
    inv_ref[...] = jnp.where(eye, 1.0, 0.0).astype(jnp.float32)
    lane = lax.broadcasted_iota(jnp.int32, (MP, BS), 1)
    sub = lax.broadcasted_iota(jnp.int32, (MP, BS), 0)
    sub_col = lax.broadcasted_iota(jnp.int32, (MP, 1), 0)
    rows = lax.broadcasted_iota(jnp.int32, (BS, 1), 0)

    for p in range(BS // MP):
        j0 = p * MP
        r = blk_ref[j0:j0 + MP, :]
        m = inv_ref[j0:j0 + MP, :]
        for t in range(MP):
            rt = r[t:t + 1, :]
            scale = lax.rsqrt(r[t:t + 1, j0 + t:j0 + t + 1])
            coef = jnp.where(sub_col > t, r[:, j0 + t:j0 + t + 1] * scale, 0.0)
            ct = jnp.where(lane[0:1, :] >= j0 + t, rt * scale, 0.0)
            r = jnp.where(sub == t, ct, r - coef * ct)
            mt = m[t:t + 1, :] * scale
            m = jnp.where(sub == t, mt, m - coef * mt)
        inv_ref[j0:j0 + MP, :] = m
        below = j0 + MP
        if below < BS:
            both = _tn(r[:, below:], jnp.concatenate([r, m], axis=1))
            blk_ref[below:, :] = blk_ref[below:, :] - both[:, :BS]
            inv_ref[below:, :] = inv_ref[below:, :] - both[:, BS:]


def _kernel(s_ref, u_ref, o_ref, a_ref, l_ref, m_ref, blk_ref, inv_ref):
    n = s_ref.shape[0]
    nb = n // BS
    a_ref[...] = s_ref[...]
    for k in range(nb):
        lo = k * BS
        blk_ref[...] = a_ref[lo:lo + BS, lo:lo + BS]
        _block_inverse(blk_ref, inv_ref)
        mkk = inv_ref[...]
        m_ref[k] = mkk
        if k + 1 < nb:
            panel = _nt(a_ref[lo + BS:, lo:lo + BS], mkk)
            l_ref[lo + BS:, lo:lo + BS] = panel
            a_ref[lo + BS:, lo + BS:] = a_ref[lo + BS:, lo + BS:] - _nt(panel, panel)
    for j in range(nb):
        lo = j * BS
        acc = u_ref[:, lo:lo + BS]
        if j > 0:
            acc = acc - _nt(o_ref[:, :lo], l_ref[lo:lo + BS, :lo])
        o_ref[:, lo:lo + BS] = _nt(acc, m_ref[j])


def factor_solve(symmetric, rows):
    n = symmetric.shape[0]
    m = rows.shape[0]
    return pl.pallas_call(
        _kernel,
        out_shape=jax.ShapeDtypeStruct((m, n), jnp.float32),
        scratch_shapes=[
            pltpu.VMEM((n, n), jnp.float32),
            pltpu.VMEM((n, n), jnp.float32),
            pltpu.VMEM((n // BS, BS, BS), jnp.float32),
            pltpu.VMEM((BS, BS), jnp.float32),
            pltpu.VMEM((BS, BS), jnp.float32),
        ],
        compiler_params=pltpu.CompilerParams(vmem_limit_bytes=60 * 1024 * 1024),
    )(symmetric, rows)


def gather_rows_col_first(rows):
    within = lax.all_gather(rows, "col", axis=0, tiled=True)
    return lax.all_gather(within, "row", axis=0, tiled=True)


def gather_rows(rows):
    n_row = lax.axis_size("row")
    n_col = lax.axis_size("col")
    across = lax.all_gather(rows, "row", axis=0, tiled=True)
    both = lax.all_gather(across, "col", axis=0, tiled=True)
    both = both.reshape(n_col, n_row, rows.shape[0], rows.shape[1])
    return both.transpose(1, 0, 2, 3).reshape(-1, rows.shape[1])


def body(
    leaf_inverse,
    leaf_coupling,
    window_coupling,
    leaf_rows,
    leaf_sizes,
    owner_table,
    schur_block,
    prior_panels,
):
    leaf_order = leaf_inverse.shape[1]
    col_width = window_coupling.shape[2]
    local_rows = schur_block.shape[0]
    group_rows = lax.axis_size("col") * local_rows
    window_rows = col_width // (lax.axis_size("row") * lax.axis_size("col"))
    position = jnp.arange(leaf_order, dtype=jnp.int32)
    active = position[None, :, None] < leaf_sizes[:, None, None]
    masked = jnp.where(active, window_coupling, jnp.zeros_like(window_coupling))
    solved = jnp.einsum("lij,ljw->liw", leaf_inverse, masked, preferred_element_type=jnp.float32)
    solved = jnp.where(active, solved, jnp.zeros_like(solved)).astype(jnp.bfloat16)
    leaf_terms = jnp.einsum(
        "lin,liw->lnw", leaf_coupling, solved, preferred_element_type=jnp.float32
    )
    block_of = leaf_rows // RB
    slots = lax.broadcasted_iota(jnp.int32, (1, 1, owner_table.shape[1]), 2)
    shift = jnp.sum(
        jnp.where(block_of[:, :, None] == slots, owner_table[0][None, None, :] - slots, 0), axis=2
    )
    targets = leaf_rows + shift * RB
    placed = jnp.zeros((group_rows, col_width), jnp.float32)
    placed = placed.at[targets.reshape(-1)].add(leaf_terms.reshape(-1, col_width))
    reduced = lax.psum_scatter(placed, "col", scatter_dimension=0, tiled=True)
    panels_win = gather_rows_col_first(prior_panels[:window_rows])
    partial = schur_block - jnp.dot(prior_panels, panels_win.T, precision=lax.Precision.HIGHEST)
    partial = lax.optimization_barrier(partial)
    updated = partial - reduced
    window_block = gather_rows(updated[:window_rows])
    symmetric = 0.5 * (window_block + window_block.T)
    return factor_solve(symmetric, updated)


def solution(mesh):
    placed = (
        P(("row", "col"), None, None),
        P(("row", "col"), None, None),
        P(("row", "col"), None, None),
        P(("row", "col"), None),
        P(("row", "col")),
        P("row", None),
        P(("row", "col"), None),
        P(("row", "col"), None),
    )
    return jax.shard_map(
        body, mesh=mesh, in_specs=placed, out_specs=P(("row", "col"), None), check_vma=False
    )
```

```python
import jax
import jax.numpy as jnp
from jax import lax
from jax.experimental import pallas as pl
from jax.experimental.pallas import tpu as pltpu
from jax.sharding import PartitionSpec as P

RB = 64
BS = 128
MP = 64
HI = lax.Precision.HIGHEST


def _nt(a, b):
    return lax.dot_general(a, b, (((1,), (1,)), ((), ())), precision=HI,
                           preferred_element_type=jnp.float32)


def _tn(a, b):
    return lax.dot_general(a, b, (((0,), (0,)), ((), ())), precision=HI,
                           preferred_element_type=jnp.float32)


def _block_inverse(blk_ref, inv_ref):
    eye = lax.broadcasted_iota(jnp.int32, (BS, BS), 0) == lax.broadcasted_iota(jnp.int32, (BS, BS), 1)
    inv_ref[...] = jnp.where(eye, 1.0, 0.0).astype(jnp.float32)
    lane = lax.broadcasted_iota(jnp.int32, (MP, BS), 1)
    sub = lax.broadcasted_iota(jnp.int32, (MP, BS), 0)
    sub_col = lax.broadcasted_iota(jnp.int32, (MP, 1), 0)
    rows = lax.broadcasted_iota(jnp.int32, (BS, 1), 0)

    for p in range(BS // MP):
        j0 = p * MP
        r = blk_ref[j0:j0 + MP, :]
        m = inv_ref[j0:j0 + MP, :]
        for t in range(MP):
            rt = r[t:t + 1, :]
            scale = lax.rsqrt(r[t:t + 1, j0 + t:j0 + t + 1])
            coef = jnp.where(sub_col > t, r[:, j0 + t:j0 + t + 1] * scale, 0.0)
            ct = jnp.where(lane[0:1, :] >= j0 + t, rt * scale, 0.0)
            r = jnp.where(sub == t, ct, r - coef * ct)
            mt = m[t:t + 1, :] * scale
            m = jnp.where(sub == t, mt, m - coef * mt)
        inv_ref[j0:j0 + MP, :] = m
        below = j0 + MP
        if below < BS:
            both = _tn(r[:, below:], jnp.concatenate([r, m], axis=1))
            blk_ref[below:, :] = blk_ref[below:, :] - both[:, :BS]
            inv_ref[below:, :] = inv_ref[below:, :] - both[:, BS:]


def _kernel(s_ref, u_ref, o_ref, a_ref, l_ref, m_ref, blk_ref, inv_ref):
    n = s_ref.shape[0]
    nb = n // BS
    a_ref[...] = s_ref[...]
    for k in range(nb):
        lo = k * BS
        blk_ref[...] = a_ref[lo:lo + BS, lo:lo + BS]
        _block_inverse(blk_ref, inv_ref)
        mkk = inv_ref[...]
        m_ref[k] = mkk
        if k + 1 < nb:
            panel = _nt(a_ref[lo + BS:, lo:lo + BS], mkk)
            l_ref[lo + BS:, lo:lo + BS] = panel
            a_ref[lo + BS:, lo + BS:] = a_ref[lo + BS:, lo + BS:] - _nt(panel, panel)
    for j in range(nb):
        lo = j * BS
        acc = u_ref[:, lo:lo + BS]
        if j > 0:
            acc = acc - _nt(o_ref[:, :lo], l_ref[lo:lo + BS, :lo])
        o_ref[:, lo:lo + BS] = _nt(acc, m_ref[j])


def factor_solve(symmetric, rows):
    n = symmetric.shape[0]
    m = rows.shape[0]
    return pl.pallas_call(
        _kernel,
        out_shape=jax.ShapeDtypeStruct((m, n), jnp.float32),
        scratch_shapes=[
            pltpu.VMEM((n, n), jnp.float32),
            pltpu.VMEM((n, n), jnp.float32),
            pltpu.VMEM((n // BS, BS, BS), jnp.float32),
            pltpu.VMEM((BS, BS), jnp.float32),
            pltpu.VMEM((BS, BS), jnp.float32),
        ],
        compiler_params=pltpu.CompilerParams(vmem_limit_bytes=60 * 1024 * 1024),
    )(symmetric, rows)


def gather_rows_col_first(rows):
    within = lax.all_gather(rows, "col", axis=0, tiled=True)
    return lax.all_gather(within, "row", axis=0, tiled=True)


def gather_rows(rows):
    n_row = lax.axis_size("row")
    n_col = lax.axis_size("col")
    across = lax.all_gather(rows, "row", axis=0, tiled=True)
    both = lax.all_gather(across, "col", axis=0, tiled=True)
    both = both.reshape(n_col, n_row, rows.shape[0], rows.shape[1])
    return both.transpose(1, 0, 2, 3).reshape(-1, rows.shape[1])


def body(
    leaf_inverse,
    leaf_coupling,
    window_coupling,
    leaf_rows,
    leaf_sizes,
    owner_table,
    schur_block,
    prior_panels,
):
    leaf_order = leaf_inverse.shape[1]
    col_width = window_coupling.shape[2]
    local_rows = schur_block.shape[0]
    group_rows = lax.axis_size("col") * local_rows
    window_rows = col_width // (lax.axis_size("row") * lax.axis_size("col"))
    position = jnp.arange(leaf_order, dtype=jnp.int32)
    active = position[None, :, None] < leaf_sizes[:, None, None]
    block_of = leaf_rows // RB
    slots = lax.broadcasted_iota(jnp.int32, (1, 1, owner_table.shape[1]), 2)
    shift = jnp.sum(
        jnp.where(block_of[:, :, None] == slots, owner_table[0][None, None, :] - slots, 0), axis=2
    )
    targets = (leaf_rows + shift * RB).reshape(-1)
    halves = []
    half_width = col_width // 2
    for half in range(2):
        part = window_coupling[:, :, half * half_width : (half + 1) * half_width]
        masked = jnp.where(active, part, jnp.zeros_like(part))
        solved = jnp.einsum("lij,ljw->liw", leaf_inverse, masked, preferred_element_type=jnp.float32)
        solved = jnp.where(active, solved, jnp.zeros_like(solved)).astype(jnp.bfloat16)
        leaf_terms = jnp.einsum(
            "lin,liw->lnw", leaf_coupling, solved, preferred_element_type=jnp.float32
        )
        placed = jnp.zeros((group_rows, half_width), jnp.float32)
        placed = placed.at[targets].add(leaf_terms.reshape(-1, half_width))
        halves.append(lax.psum_scatter(placed, "col", scatter_dimension=0, tiled=True))
    reduced = jnp.concatenate(halves, axis=1)
    panels_win = gather_rows_col_first(prior_panels[:window_rows])
    partial = schur_block - jnp.dot(prior_panels, panels_win.T, precision=lax.Precision.HIGHEST)
    partial = lax.optimization_barrier(partial)
    updated = partial - reduced
    window_block = gather_rows(updated[:window_rows])
    symmetric = 0.5 * (window_block + window_block.T)
    return factor_solve(symmetric, updated)


def solution(mesh):
    placed = (
        P(("row", "col"), None, None),
        P(("row", "col"), None, None),
        P(("row", "col"), None, None),
        P(("row", "col"), None),
        P(("row", "col")),
        P("row", None),
        P(("row", "col"), None),
        P(("row", "col"), None),
    )
    return jax.shard_map(
        body, mesh=mesh, in_specs=placed, out_specs=P(("row", "col"), None), check_vma=False
    )
```

```python
import jax
import jax.numpy as jnp
from jax import lax
from jax.experimental import pallas as pl
from jax.experimental.pallas import tpu as pltpu
from jax.sharding import PartitionSpec as P

RB = 64
BS = 128
MP = 64
HI = lax.Precision.HIGHEST


def _nt(a, b):
    return lax.dot_general(a, b, (((1,), (1,)), ((), ())), precision=HI,
                           preferred_element_type=jnp.float32)


def _tn(a, b):
    return lax.dot_general(a, b, (((0,), (0,)), ((), ())), precision=HI,
                           preferred_element_type=jnp.float32)


def _block_inverse(blk_ref, inv_ref):
    eye = lax.broadcasted_iota(jnp.int32, (BS, BS), 0) == lax.broadcasted_iota(jnp.int32, (BS, BS), 1)
    inv_ref[...] = jnp.where(eye, 1.0, 0.0).astype(jnp.float32)
    lane = lax.broadcasted_iota(jnp.int32, (MP, BS), 1)
    sub = lax.broadcasted_iota(jnp.int32, (MP, BS), 0)
    sub_col = lax.broadcasted_iota(jnp.int32, (MP, 1), 0)
    rows = lax.broadcasted_iota(jnp.int32, (BS, 1), 0)

    for p in range(BS // MP):
        j0 = p * MP
        r = blk_ref[j0:j0 + MP, :]
        m = inv_ref[j0:j0 + MP, :]
        for t in range(MP):
            rt = r[t:t + 1, :]
            scale = lax.rsqrt(r[t:t + 1, j0 + t:j0 + t + 1])
            coef = jnp.where(sub_col > t, r[:, j0 + t:j0 + t + 1] * scale, 0.0)
            ct = jnp.where(lane[0:1, :] >= j0 + t, rt * scale, 0.0)
            r = jnp.where(sub == t, ct, r - coef * ct)
            mt = m[t:t + 1, :] * scale
            m = jnp.where(sub == t, mt, m - coef * mt)
        inv_ref[j0:j0 + MP, :] = m
        below = j0 + MP
        if below < BS:
            both = _tn(r[:, below:], jnp.concatenate([r, m], axis=1))
            blk_ref[below:, :] = blk_ref[below:, :] - both[:, :BS]
            inv_ref[below:, :] = inv_ref[below:, :] - both[:, BS:]


def _kernel(s_ref, u_ref, o_ref, a_ref, l_ref, m_ref, blk_ref, inv_ref):
    n = s_ref.shape[0]
    nb = n // BS
    a_ref[...] = s_ref[...]
    for k in range(nb):
        lo = k * BS
        blk_ref[...] = a_ref[lo:lo + BS, lo:lo + BS]
        _block_inverse(blk_ref, inv_ref)
        mkk = inv_ref[...]
        m_ref[k] = mkk
        if k + 1 < nb:
            panel = _nt(a_ref[lo + BS:, lo:lo + BS], mkk)
            l_ref[lo + BS:, lo:lo + BS] = panel
            a_ref[lo + BS:, lo + BS:] = a_ref[lo + BS:, lo + BS:] - _nt(panel, panel)
    for j in range(nb):
        lo = j * BS
        acc = u_ref[:, lo:lo + BS]
        if j > 0:
            acc = acc - _nt(o_ref[:, :lo], l_ref[lo:lo + BS, :lo])
        o_ref[:, lo:lo + BS] = _nt(acc, m_ref[j])


def factor_solve(symmetric, rows):
    n = symmetric.shape[0]
    m = rows.shape[0]
    return pl.pallas_call(
        _kernel,
        out_shape=jax.ShapeDtypeStruct((m, n), jnp.float32),
        scratch_shapes=[
            pltpu.VMEM((n, n), jnp.float32),
            pltpu.VMEM((n, n), jnp.float32),
            pltpu.VMEM((n // BS, BS, BS), jnp.float32),
            pltpu.VMEM((BS, BS), jnp.float32),
            pltpu.VMEM((BS, BS), jnp.float32),
        ],
        compiler_params=pltpu.CompilerParams(vmem_limit_bytes=60 * 1024 * 1024),
    )(symmetric, rows)


def gather_small(rows, axis):
    count = lax.axis_size(axis)
    shifted = [rows]
    for step in range(1, count):
        pairs = [(i, (i + step) % count) for i in range(count)]
        shifted.append(lax.ppermute(rows, axis, pairs))
    stacked = jnp.stack(shifted)
    order = (lax.axis_index(axis) - jnp.arange(count, dtype=jnp.int32)) % count
    return jnp.take(stacked, order, axis=0).reshape(-1, rows.shape[1])


def gather_rows_col_first(rows):
    within = gather_small(rows, "col")
    return lax.all_gather(within, "row", axis=0, tiled=True)


def gather_rows(rows):
    n_row = lax.axis_size("row")
    n_col = lax.axis_size("col")
    across = gather_small(rows, "row")
    both = lax.all_gather(across, "col", axis=0, tiled=True)
    both = both.reshape(n_col, n_row, rows.shape[0], rows.shape[1])
    return both.transpose(1, 0, 2, 3).reshape(-1, rows.shape[1])


def body(
    leaf_inverse,
    leaf_coupling,
    window_coupling,
    leaf_rows,
    leaf_sizes,
    owner_table,
    schur_block,
    prior_panels,
):
    leaf_order = leaf_inverse.shape[1]
    col_width = window_coupling.shape[2]
    local_rows = schur_block.shape[0]
    group_rows = lax.axis_size("col") * local_rows
    window_rows = col_width // (lax.axis_size("row") * lax.axis_size("col"))
    position = jnp.arange(leaf_order, dtype=jnp.int32)
    active = position[None, :, None] < leaf_sizes[:, None, None]
    masked = jnp.where(active, window_coupling, jnp.zeros_like(window_coupling))
    solved = jnp.einsum("lij,ljw->liw", leaf_inverse, masked, preferred_element_type=jnp.float32)
    solved = jnp.where(active, solved, jnp.zeros_like(solved)).astype(jnp.bfloat16)
    leaf_terms = jnp.einsum(
        "lin,liw->lnw", leaf_coupling, solved, preferred_element_type=jnp.float32
    )
    block_of = leaf_rows // RB
    slots = lax.broadcasted_iota(jnp.int32, (1, 1, owner_table.shape[1]), 2)
    shift = jnp.sum(
        jnp.where(block_of[:, :, None] == slots, owner_table[0][None, None, :] - slots, 0), axis=2
    )
    targets = leaf_rows + shift * RB
    placed = jnp.zeros((group_rows, col_width), jnp.float32)
    placed = placed.at[targets.reshape(-1)].add(leaf_terms.reshape(-1, col_width))
    reduced = lax.psum_scatter(placed, "col", scatter_dimension=0, tiled=True)
    panels_win = gather_rows_col_first(prior_panels[:window_rows])
    partial = schur_block - jnp.dot(prior_panels, panels_win.T, precision=lax.Precision.HIGHEST)
    partial = lax.optimization_barrier(partial)
    updated = partial - reduced
    window_block = gather_rows(updated[:window_rows])
    symmetric = 0.5 * (window_block + window_block.T)
    return factor_solve(symmetric, updated)


def solution(mesh):
    placed = (
        P(("row", "col"), None, None),
        P(("row", "col"), None, None),
        P(("row", "col"), None, None),
        P(("row", "col"), None),
        P(("row", "col")),
        P("row", None),
        P(("row", "col"), None),
        P(("row", "col"), None),
    )
    return jax.shard_map(
        body, mesh=mesh, in_specs=placed, out_specs=P(("row", "col"), None), check_vma=False
    )
```

```python
import jax
import jax.numpy as jnp
from jax import lax
from jax.experimental import pallas as pl
from jax.experimental.pallas import tpu as pltpu
from jax.sharding import PartitionSpec as P

RB = 64
BS = 128
MP = 64
HI = lax.Precision.HIGHEST


def _nt(a, b):
    return lax.dot_general(a, b, (((1,), (1,)), ((), ())), precision=HI,
                           preferred_element_type=jnp.float32)


def _tn(a, b):
    return lax.dot_general(a, b, (((0,), (0,)), ((), ())), precision=HI,
                           preferred_element_type=jnp.float32)


def _block_inverse(blk_ref, inv_ref):
    eye = lax.broadcasted_iota(jnp.int32, (BS, BS), 0) == lax.broadcasted_iota(jnp.int32, (BS, BS), 1)
    inv_ref[...] = jnp.where(eye, 1.0, 0.0).astype(jnp.float32)
    lane = lax.broadcasted_iota(jnp.int32, (MP, BS), 1)
    sub = lax.broadcasted_iota(jnp.int32, (MP, BS), 0)
    sub_col = lax.broadcasted_iota(jnp.int32, (MP, 1), 0)
    rows = lax.broadcasted_iota(jnp.int32, (BS, 1), 0)

    for p in range(BS // MP):
        j0 = p * MP
        r = blk_ref[j0:j0 + MP, :]
        m = inv_ref[j0:j0 + MP, :]
        for t in range(MP):
            rt = r[t:t + 1, :]
            scale = lax.rsqrt(r[t:t + 1, j0 + t:j0 + t + 1])
            coef = jnp.where(sub_col > t, r[:, j0 + t:j0 + t + 1] * scale, 0.0)
            ct = jnp.where(lane[0:1, :] >= j0 + t, rt * scale, 0.0)
            r = jnp.where(sub == t, ct, r - coef * ct)
            mt = m[t:t + 1, :] * scale
            m = jnp.where(sub == t, mt, m - coef * mt)
        inv_ref[j0:j0 + MP, :] = m
        below = j0 + MP
        if below < BS:
            both = _tn(r[:, below:], jnp.concatenate([r, m], axis=1))
            blk_ref[below:, :] = blk_ref[below:, :] - both[:, :BS]
            inv_ref[below:, :] = inv_ref[below:, :] - both[:, BS:]


def _kernel(s_ref, u_ref, o_ref, a_ref, l_ref, m_ref, blk_ref, inv_ref):
    n = s_ref.shape[0]
    nb = n // BS
    a_ref[...] = s_ref[...]
    for k in range(nb):
        lo = k * BS
        blk_ref[...] = a_ref[lo:lo + BS, lo:lo + BS]
        _block_inverse(blk_ref, inv_ref)
        mkk = inv_ref[...]
        m_ref[k] = mkk
        if k + 1 < nb:
            panel = _nt(a_ref[lo + BS:, lo:lo + BS], mkk)
            l_ref[lo + BS:, lo:lo + BS] = panel
            a_ref[lo + BS:, lo + BS:] = a_ref[lo + BS:, lo + BS:] - _nt(panel, panel)
    for j in range(nb):
        lo = j * BS
        acc = u_ref[:, lo:lo + BS]
        if j > 0:
            acc = acc - _nt(o_ref[:, :lo], l_ref[lo:lo + BS, :lo])
        o_ref[:, lo:lo + BS] = _nt(acc, m_ref[j])


def factor_solve(symmetric, rows):
    n = symmetric.shape[0]
    m = rows.shape[0]
    return pl.pallas_call(
        _kernel,
        out_shape=jax.ShapeDtypeStruct((m, n), jnp.float32),
        scratch_shapes=[
            pltpu.VMEM((n, n), jnp.float32),
            pltpu.VMEM((n, n), jnp.float32),
            pltpu.VMEM((n // BS, BS, BS), jnp.float32),
            pltpu.VMEM((BS, BS), jnp.float32),
            pltpu.VMEM((BS, BS), jnp.float32),
        ],
        compiler_params=pltpu.CompilerParams(vmem_limit_bytes=60 * 1024 * 1024),
    )(symmetric, rows)


def gather_small(rows, axis):
    count = lax.axis_size(axis)
    shifted = [rows]
    for step in range(1, count):
        pairs = [(i, (i + step) % count) for i in range(count)]
        shifted.append(lax.ppermute(rows, axis, pairs))
    stacked = jnp.stack(shifted)
    order = (lax.axis_index(axis) - jnp.arange(count, dtype=jnp.int32)) % count
    return jnp.take(stacked, order, axis=0).reshape(-1, rows.shape[1])


def gather_rows_col_first(rows, alongside):
    within = gather_small(rows, "col")
    within, alongside = lax.optimization_barrier((within, alongside))
    return lax.all_gather(within, "row", axis=0, tiled=True), alongside


def gather_rows(rows):
    n_row = lax.axis_size("row")
    n_col = lax.axis_size("col")
    across = gather_small(rows, "row")
    both = lax.all_gather(across, "col", axis=0, tiled=True)
    both = both.reshape(n_col, n_row, rows.shape[0], rows.shape[1])
    return both.transpose(1, 0, 2, 3).reshape(-1, rows.shape[1])


def body(
    leaf_inverse,
    leaf_coupling,
    window_coupling,
    leaf_rows,
    leaf_sizes,
    owner_table,
    schur_block,
    prior_panels,
):
    leaf_order = leaf_inverse.shape[1]
    col_width = window_coupling.shape[2]
    local_rows = schur_block.shape[0]
    group_rows = lax.axis_size("col") * local_rows
    window_rows = col_width // (lax.axis_size("row") * lax.axis_size("col"))
    position = jnp.arange(leaf_order, dtype=jnp.int32)
    active = position[None, :, None] < leaf_sizes[:, None, None]
    masked = jnp.where(active, window_coupling, jnp.zeros_like(window_coupling))
    solved = jnp.einsum("lij,ljw->liw", leaf_inverse, masked, preferred_element_type=jnp.float32)
    solved = jnp.where(active, solved, jnp.zeros_like(solved)).astype(jnp.bfloat16)
    leaf_terms = jnp.einsum(
        "lin,liw->lnw", leaf_coupling, solved, preferred_element_type=jnp.float32
    )
    block_of = leaf_rows // RB
    slots = lax.broadcasted_iota(jnp.int32, (1, 1, owner_table.shape[1]), 2)
    shift = jnp.sum(
        jnp.where(block_of[:, :, None] == slots, owner_table[0][None, None, :] - slots, 0), axis=2
    )
    targets = leaf_rows + shift * RB
    placed = jnp.zeros((group_rows, col_width), jnp.float32)
    placed = placed.at[targets.reshape(-1)].add(leaf_terms.reshape(-1, col_width))
    panels_win, placed = gather_rows_col_first(prior_panels[:window_rows], placed)
    reduced = lax.psum_scatter(placed, "col", scatter_dimension=0, tiled=True)
    partial = schur_block - jnp.dot(prior_panels, panels_win.T, precision=lax.Precision.HIGHEST)
    partial = lax.optimization_barrier(partial)
    updated = partial - reduced
    window_block = gather_rows(updated[:window_rows])
    symmetric = 0.5 * (window_block + window_block.T)
    return factor_solve(symmetric, updated)


def solution(mesh):
    placed = (
        P(("row", "col"), None, None),
        P(("row", "col"), None, None),
        P(("row", "col"), None, None),
        P(("row", "col"), None),
        P(("row", "col")),
        P("row", None),
        P(("row", "col"), None),
        P(("row", "col"), None),
    )
    return jax.shard_map(
        body, mesh=mesh, in_specs=placed, out_specs=P(("row", "col"), None), check_vma=False
    )
```

```python
import jax
import jax.numpy as jnp
from jax import lax
from jax.experimental import pallas as pl
from jax.experimental.pallas import tpu as pltpu
from jax.sharding import PartitionSpec as P

RB = 64
BS = 128
MP = 64
HI = lax.Precision.HIGHEST


def _nt(a, b):
    return lax.dot_general(a, b, (((1,), (1,)), ((), ())), precision=HI,
                           preferred_element_type=jnp.float32)


def _tn(a, b):
    return lax.dot_general(a, b, (((0,), (0,)), ((), ())), precision=HI,
                           preferred_element_type=jnp.float32)


def _block_inverse(blk_ref, inv_ref):
    eye = lax.broadcasted_iota(jnp.int32, (BS, BS), 0) == lax.broadcasted_iota(jnp.int32, (BS, BS), 1)
    inv_ref[...] = jnp.where(eye, 1.0, 0.0).astype(jnp.float32)
    lane = lax.broadcasted_iota(jnp.int32, (MP, BS), 1)
    sub = lax.broadcasted_iota(jnp.int32, (MP, BS), 0)
    sub_col = lax.broadcasted_iota(jnp.int32, (MP, 1), 0)
    rows = lax.broadcasted_iota(jnp.int32, (BS, 1), 0)

    for p in range(BS // MP):
        j0 = p * MP
        r = blk_ref[j0:j0 + MP, :]
        m = inv_ref[j0:j0 + MP, :]
        for t in range(MP):
            rt = r[t:t + 1, :]
            scale = lax.rsqrt(r[t:t + 1, j0 + t:j0 + t + 1])
            coef = jnp.where(sub_col > t, r[:, j0 + t:j0 + t + 1] * scale, 0.0)
            ct = jnp.where(lane[0:1, :] >= j0 + t, rt * scale, 0.0)
            r = jnp.where(sub == t, ct, r - coef * ct)
            mt = m[t:t + 1, :] * scale
            m = jnp.where(sub == t, mt, m - coef * mt)
        inv_ref[j0:j0 + MP, :] = m
        below = j0 + MP
        if below < BS:
            both = _tn(r[:, below:], jnp.concatenate([r, m], axis=1))
            blk_ref[below:, :] = blk_ref[below:, :] - both[:, :BS]
            inv_ref[below:, :] = inv_ref[below:, :] - both[:, BS:]


def _kernel(s_ref, u_ref, o_ref, a_ref, l_ref, m_ref, blk_ref, inv_ref):
    n = s_ref.shape[0]
    nb = n // BS
    a_ref[...] = s_ref[...]
    for k in range(nb):
        lo = k * BS
        blk_ref[...] = a_ref[lo:lo + BS, lo:lo + BS]
        _block_inverse(blk_ref, inv_ref)
        mkk = inv_ref[...]
        m_ref[k] = mkk
        if k + 1 < nb:
            panel = _nt(a_ref[lo + BS:, lo:lo + BS], mkk)
            l_ref[lo + BS:, lo:lo + BS] = panel
            a_ref[lo + BS:, lo + BS:] = a_ref[lo + BS:, lo + BS:] - _nt(panel, panel)
    for j in range(nb):
        lo = j * BS
        acc = u_ref[:, lo:lo + BS]
        if j > 0:
            acc = acc - _nt(o_ref[:, :lo], l_ref[lo:lo + BS, :lo])
        o_ref[:, lo:lo + BS] = _nt(acc, m_ref[j])


def factor_solve(symmetric, rows):
    n = symmetric.shape[0]
    m = rows.shape[0]
    return pl.pallas_call(
        _kernel,
        out_shape=jax.ShapeDtypeStruct((m, n), jnp.float32),
        scratch_shapes=[
            pltpu.VMEM((n, n), jnp.float32),
            pltpu.VMEM((n, n), jnp.float32),
            pltpu.VMEM((n // BS, BS, BS), jnp.float32),
            pltpu.VMEM((BS, BS), jnp.float32),
            pltpu.VMEM((BS, BS), jnp.float32),
        ],
        compiler_params=pltpu.CompilerParams(vmem_limit_bytes=60 * 1024 * 1024),
    )(symmetric, rows)


def gather_small(rows, axis):
    count = lax.axis_size(axis)
    shifted = [rows]
    for step in range(1, count):
        pairs = [(i, (i + step) % count) for i in range(count)]
        shifted.append(lax.ppermute(rows, axis, pairs))
    stacked = jnp.stack(shifted)
    order = (lax.axis_index(axis) - jnp.arange(count, dtype=jnp.int32)) % count
    return jnp.take(stacked, order, axis=0).reshape(-1, rows.shape[1])


def gather_rows(rows):
    n_row = lax.axis_size("row")
    n_col = lax.axis_size("col")
    across = gather_small(rows, "row")
    both = lax.all_gather(across, "col", axis=0, tiled=True)
    both = both.reshape(n_col, n_row, rows.shape[0], rows.shape[1])
    return both.transpose(1, 0, 2, 3).reshape(-1, rows.shape[1])


def body(
    leaf_inverse,
    leaf_coupling,
    window_coupling,
    leaf_rows,
    leaf_sizes,
    owner_table,
    schur_block,
    prior_panels,
):
    leaf_order = leaf_inverse.shape[1]
    col_width = window_coupling.shape[2]
    local_rows = schur_block.shape[0]
    group_rows = lax.axis_size("col") * local_rows
    window_rows = col_width // (lax.axis_size("row") * lax.axis_size("col"))
    position = jnp.arange(leaf_order, dtype=jnp.int32)
    active = position[None, :, None] < leaf_sizes[:, None, None]
    masked = jnp.where(active, window_coupling, jnp.zeros_like(window_coupling))
    solved = jnp.einsum("lij,ljw->liw", leaf_inverse, masked, preferred_element_type=jnp.float32)
    solved = jnp.where(active, solved, jnp.zeros_like(solved)).astype(jnp.bfloat16)
    leaf_terms = jnp.einsum(
        "lin,liw->lnw", leaf_coupling, solved, preferred_element_type=jnp.float32
    )
    block_of = leaf_rows // RB
    slots = lax.broadcasted_iota(jnp.int32, (1, 1, owner_table.shape[1]), 2)
    shift = jnp.sum(
        jnp.where(block_of[:, :, None] == slots, owner_table[0][None, None, :] - slots, 0), axis=2
    )
    targets = leaf_rows + shift * RB
    placed = jnp.zeros((group_rows, col_width), jnp.float32)
    placed = placed.at[targets.reshape(-1)].add(leaf_terms.reshape(-1, col_width))
    reduced = lax.psum_scatter(placed, "col", scatter_dimension=0, tiled=True)
    panels_win = gather_rows(prior_panels[:window_rows])
    partial = schur_block - jnp.dot(prior_panels, panels_win.T, precision=lax.Precision.HIGHEST)
    partial = lax.optimization_barrier(partial)
    updated = partial - reduced
    window_block = gather_rows(updated[:window_rows])
    symmetric = 0.5 * (window_block + window_block.T)
    return factor_solve(symmetric, updated)


def solution(mesh):
    placed = (
        P(("row", "col"), None, None),
        P(("row", "col"), None, None),
        P(("row", "col"), None, None),
        P(("row", "col"), None),
        P(("row", "col")),
        P("row", None),
        P(("row", "col"), None),
        P(("row", "col"), None),
    )
    return jax.shard_map(
        body, mesh=mesh, in_specs=placed, out_specs=P(("row", "col"), None), check_vma=False
    )
```

```python
import jax
import jax.numpy as jnp
from jax import lax
from jax.experimental import pallas as pl
from jax.experimental.pallas import tpu as pltpu
from jax.sharding import PartitionSpec as P

RB = 64
BS = 128
MP = 64
HI = lax.Precision.HIGHEST


def _nt(a, b):
    return lax.dot_general(a, b, (((1,), (1,)), ((), ())), precision=HI,
                           preferred_element_type=jnp.float32)


def _tn(a, b):
    return lax.dot_general(a, b, (((0,), (0,)), ((), ())), precision=HI,
                           preferred_element_type=jnp.float32)


def _block_inverse(blk_ref, inv_ref):
    eye = lax.broadcasted_iota(jnp.int32, (BS, BS), 0) == lax.broadcasted_iota(jnp.int32, (BS, BS), 1)
    inv_ref[...] = jnp.where(eye, 1.0, 0.0).astype(jnp.float32)
    lane = lax.broadcasted_iota(jnp.int32, (MP, BS), 1)
    sub = lax.broadcasted_iota(jnp.int32, (MP, BS), 0)
    sub_col = lax.broadcasted_iota(jnp.int32, (MP, 1), 0)
    rows = lax.broadcasted_iota(jnp.int32, (BS, 1), 0)

    for p in range(BS // MP):
        j0 = p * MP
        r = blk_ref[j0:j0 + MP, :]
        m = inv_ref[j0:j0 + MP, :]
        for t in range(MP):
            rt = r[t:t + 1, :]
            scale = lax.rsqrt(r[t:t + 1, j0 + t:j0 + t + 1])
            coef = jnp.where(sub_col > t, r[:, j0 + t:j0 + t + 1] * scale, 0.0)
            ct = jnp.where(lane[0:1, :] >= j0 + t, rt * scale, 0.0)
            r = jnp.where(sub == t, ct, r - coef * ct)
            mt = m[t:t + 1, :] * scale
            m = jnp.where(sub == t, mt, m - coef * mt)
        inv_ref[j0:j0 + MP, :] = m
        below = j0 + MP
        if below < BS:
            both = _tn(r[:, below:], jnp.concatenate([r, m], axis=1))
            blk_ref[below:, :] = blk_ref[below:, :] - both[:, :BS]
            inv_ref[below:, :] = inv_ref[below:, :] - both[:, BS:]


def _kernel(s_ref, u_ref, o_ref, a_ref, l_ref, m_ref, blk_ref, inv_ref):
    n = s_ref.shape[0]
    nb = n // BS
    for bi in range(nb):
        for bj in range(bi + 1):
            rows_i = slice(bi * BS, (bi + 1) * BS)
            rows_j = slice(bj * BS, (bj + 1) * BS)
            tile = 0.5 * (s_ref[rows_i, rows_j] + jnp.transpose(s_ref[rows_j, rows_i]))
            a_ref[rows_i, rows_j] = tile
            if bj != bi:
                a_ref[rows_j, rows_i] = jnp.transpose(tile)
    for k in range(nb):
        lo = k * BS
        blk_ref[...] = a_ref[lo:lo + BS, lo:lo + BS]
        _block_inverse(blk_ref, inv_ref)
        mkk = inv_ref[...]
        m_ref[k] = mkk
        if k + 1 < nb:
            panel = _nt(a_ref[lo + BS:, lo:lo + BS], mkk)
            l_ref[lo + BS:, lo:lo + BS] = panel
            a_ref[lo + BS:, lo + BS:] = a_ref[lo + BS:, lo + BS:] - _nt(panel, panel)
    for j in range(nb):
        lo = j * BS
        acc = u_ref[:, lo:lo + BS]
        if j > 0:
            acc = acc - _nt(o_ref[:, :lo], l_ref[lo:lo + BS, :lo])
        o_ref[:, lo:lo + BS] = _nt(acc, m_ref[j])


def factor_solve(symmetric, rows):
    n = symmetric.shape[0]
    m = rows.shape[0]
    return pl.pallas_call(
        _kernel,
        out_shape=jax.ShapeDtypeStruct((m, n), jnp.float32),
        scratch_shapes=[
            pltpu.VMEM((n, n), jnp.float32),
            pltpu.VMEM((n, n), jnp.float32),
            pltpu.VMEM((n // BS, BS, BS), jnp.float32),
            pltpu.VMEM((BS, BS), jnp.float32),
            pltpu.VMEM((BS, BS), jnp.float32),
        ],
        compiler_params=pltpu.CompilerParams(vmem_limit_bytes=60 * 1024 * 1024),
    )(symmetric, rows)


def gather_small(rows, axis):
    count = lax.axis_size(axis)
    shifted = [rows]
    for step in range(1, count):
        pairs = [(i, (i + step) % count) for i in range(count)]
        shifted.append(lax.ppermute(rows, axis, pairs))
    stacked = jnp.stack(shifted)
    order = (lax.axis_index(axis) - jnp.arange(count, dtype=jnp.int32)) % count
    return jnp.take(stacked, order, axis=0).reshape(-1, rows.shape[1])


def gather_rows(rows):
    n_row = lax.axis_size("row")
    n_col = lax.axis_size("col")
    across = gather_small(rows, "row")
    both = lax.all_gather(across, "col", axis=0, tiled=True)
    both = both.reshape(n_col, n_row, rows.shape[0], rows.shape[1])
    return both.transpose(1, 0, 2, 3).reshape(-1, rows.shape[1])


def body(
    leaf_inverse,
    leaf_coupling,
    window_coupling,
    leaf_rows,
    leaf_sizes,
    owner_table,
    schur_block,
    prior_panels,
):
    leaf_order = leaf_inverse.shape[1]
    col_width = window_coupling.shape[2]
    local_rows = schur_block.shape[0]
    group_rows = lax.axis_size("col") * local_rows
    window_rows = col_width // (lax.axis_size("row") * lax.axis_size("col"))
    position = jnp.arange(leaf_order, dtype=jnp.int32)
    active = position[None, :, None] < leaf_sizes[:, None, None]
    masked = jnp.where(active, window_coupling, jnp.zeros_like(window_coupling))
    solved = jnp.einsum("lij,ljw->liw", leaf_inverse, masked, preferred_element_type=jnp.float32)
    solved = jnp.where(active, solved, jnp.zeros_like(solved)).astype(jnp.bfloat16)
    leaf_terms = jnp.einsum(
        "lin,liw->lnw", leaf_coupling, solved, preferred_element_type=jnp.float32
    )
    block_of = leaf_rows // RB
    slots = lax.broadcasted_iota(jnp.int32, (1, 1, owner_table.shape[1]), 2)
    shift = jnp.sum(
        jnp.where(block_of[:, :, None] == slots, owner_table[0][None, None, :] - slots, 0), axis=2
    )
    targets = leaf_rows + shift * RB
    placed = jnp.zeros((group_rows, col_width), jnp.float32)
    placed = placed.at[targets.reshape(-1)].add(leaf_terms.reshape(-1, col_width))
    reduced = lax.psum_scatter(placed, "col", scatter_dimension=0, tiled=True)
    panels_win = gather_rows(prior_panels[:window_rows])
    partial = schur_block - jnp.dot(prior_panels, panels_win.T, precision=lax.Precision.HIGHEST)
    partial = lax.optimization_barrier(partial)
    updated = partial - reduced
    window_block = gather_rows(updated[:window_rows])
    return factor_solve(window_block, updated)


def solution(mesh):
    placed = (
        P(("row", "col"), None, None),
        P(("row", "col"), None, None),
        P(("row", "col"), None, None),
        P(("row", "col"), None),
        P(("row", "col")),
        P("row", None),
        P(("row", "col"), None),
        P(("row", "col"), None),
    )
    return jax.shard_map(
        body, mesh=mesh, in_specs=placed, out_specs=P(("row", "col"), None), check_vma=False
    )
```

```python
import functools

import jax
import jax.numpy as jnp
from jax import lax
from jax.experimental import pallas as pl
from jax.experimental.pallas import tpu as pltpu
from jax.sharding import PartitionSpec as P

RB = 64
BS = 128
MP = 64
HI = lax.Precision.HIGHEST


def _nt(a, b):
    return lax.dot_general(a, b, (((1,), (1,)), ((), ())), precision=HI,
                           preferred_element_type=jnp.float32)


def _tn(a, b):
    return lax.dot_general(a, b, (((0,), (0,)), ((), ())), precision=HI,
                           preferred_element_type=jnp.float32)


def _block_inverse(blk_ref, inv_ref):
    eye = lax.broadcasted_iota(jnp.int32, (BS, BS), 0) == lax.broadcasted_iota(jnp.int32, (BS, BS), 1)
    inv_ref[...] = jnp.where(eye, 1.0, 0.0).astype(jnp.float32)
    lane = lax.broadcasted_iota(jnp.int32, (MP, BS), 1)
    sub = lax.broadcasted_iota(jnp.int32, (MP, BS), 0)
    sub_col = lax.broadcasted_iota(jnp.int32, (MP, 1), 0)
    rows = lax.broadcasted_iota(jnp.int32, (BS, 1), 0)

    for p in range(BS // MP):
        j0 = p * MP
        r = blk_ref[j0:j0 + MP, :]
        m = inv_ref[j0:j0 + MP, :]
        for t in range(MP):
            rt = r[t:t + 1, :]
            scale = lax.rsqrt(r[t:t + 1, j0 + t:j0 + t + 1])
            coef = jnp.where(sub_col > t, r[:, j0 + t:j0 + t + 1] * scale, 0.0)
            ct = jnp.where(lane[0:1, :] >= j0 + t, rt * scale, 0.0)
            r = jnp.where(sub == t, ct, r - coef * ct)
            mt = m[t:t + 1, :] * scale
            m = jnp.where(sub == t, mt, m - coef * mt)
        inv_ref[j0:j0 + MP, :] = m
        below = j0 + MP
        if below < BS:
            both = _tn(r[:, below:], jnp.concatenate([r, m], axis=1))
            blk_ref[below:, :] = blk_ref[below:, :] - both[:, :BS]
            inv_ref[below:, :] = inv_ref[below:, :] - both[:, BS:]


def _kernel(n_row, n_col, s_ref, u_ref, o_ref, a_ref, l_ref, m_ref, blk_ref, inv_ref, w_ref):
    n = s_ref.shape[0]
    nb = n // BS
    piece = n // (n_row * n_col)
    for r in range(n_row):
        for c in range(n_col):
            dst = (r * n_col + c) * piece
            src = (c * n_row + r) * piece
            w_ref[dst:dst + piece, :] = s_ref[src:src + piece, :]
    for bi in range(nb):
        for bj in range(bi + 1):
            rows_i = slice(bi * BS, (bi + 1) * BS)
            rows_j = slice(bj * BS, (bj + 1) * BS)
            tile = 0.5 * (w_ref[rows_i, rows_j] + jnp.transpose(w_ref[rows_j, rows_i]))
            a_ref[rows_i, rows_j] = tile
            if bj != bi:
                a_ref[rows_j, rows_i] = jnp.transpose(tile)
    for k in range(nb):
        lo = k * BS
        blk_ref[...] = a_ref[lo:lo + BS, lo:lo + BS]
        _block_inverse(blk_ref, inv_ref)
        mkk = inv_ref[...]
        m_ref[k] = mkk
        if k + 1 < nb:
            panel = _nt(a_ref[lo + BS:, lo:lo + BS], mkk)
            l_ref[lo + BS:, lo:lo + BS] = panel
            a_ref[lo + BS:, lo + BS:] = a_ref[lo + BS:, lo + BS:] - _nt(panel, panel)
    for j in range(nb):
        lo = j * BS
        acc = u_ref[:, lo:lo + BS]
        if j > 0:
            acc = acc - _nt(o_ref[:, :lo], l_ref[lo:lo + BS, :lo])
        o_ref[:, lo:lo + BS] = _nt(acc, m_ref[j])


def factor_solve(symmetric, rows, n_row, n_col):
    n = symmetric.shape[0]
    m = rows.shape[0]
    return pl.pallas_call(
        functools.partial(_kernel, n_row, n_col),
        out_shape=jax.ShapeDtypeStruct((m, n), jnp.float32),
        scratch_shapes=[
            pltpu.VMEM((n, n), jnp.float32),
            pltpu.VMEM((n, n), jnp.float32),
            pltpu.VMEM((n // BS, BS, BS), jnp.float32),
            pltpu.VMEM((BS, BS), jnp.float32),
            pltpu.VMEM((BS, BS), jnp.float32),
            pltpu.VMEM((n, n), jnp.float32),
        ],
        compiler_params=pltpu.CompilerParams(vmem_limit_bytes=60 * 1024 * 1024),
    )(symmetric, rows)


def gather_small(rows, axis):
    count = lax.axis_size(axis)
    shifted = [rows]
    for step in range(1, count):
        pairs = [(i, (i + step) % count) for i in range(count)]
        shifted.append(lax.ppermute(rows, axis, pairs))
    stacked = jnp.stack(shifted)
    order = (lax.axis_index(axis) - jnp.arange(count, dtype=jnp.int32)) % count
    return jnp.take(stacked, order, axis=0).reshape(-1, rows.shape[1])


def gather_rows_source_order(rows):
    across = gather_small(rows, "row")
    return lax.all_gather(across, "col", axis=0, tiled=True)


def gather_rows(rows):
    n_row = lax.axis_size("row")
    n_col = lax.axis_size("col")
    across = gather_small(rows, "row")
    both = lax.all_gather(across, "col", axis=0, tiled=True)
    both = both.reshape(n_col, n_row, rows.shape[0], rows.shape[1])
    return both.transpose(1, 0, 2, 3).reshape(-1, rows.shape[1])


def body(
    leaf_inverse,
    leaf_coupling,
    window_coupling,
    leaf_rows,
    leaf_sizes,
    owner_table,
    schur_block,
    prior_panels,
):
    leaf_order = leaf_inverse.shape[1]
    col_width = window_coupling.shape[2]
    local_rows = schur_block.shape[0]
    group_rows = lax.axis_size("col") * local_rows
    window_rows = col_width // (lax.axis_size("row") * lax.axis_size("col"))
    position = jnp.arange(leaf_order, dtype=jnp.int32)
    active = position[None, :, None] < leaf_sizes[:, None, None]
    masked = jnp.where(active, window_coupling, jnp.zeros_like(window_coupling))
    solved = jnp.einsum("lij,ljw->liw", leaf_inverse, masked, preferred_element_type=jnp.float32)
    solved = jnp.where(active, solved, jnp.zeros_like(solved)).astype(jnp.bfloat16)
    leaf_terms = jnp.einsum(
        "lin,liw->lnw", leaf_coupling, solved, preferred_element_type=jnp.float32
    )
    block_of = leaf_rows // RB
    slots = lax.broadcasted_iota(jnp.int32, (1, 1, owner_table.shape[1]), 2)
    shift = jnp.sum(
        jnp.where(block_of[:, :, None] == slots, owner_table[0][None, None, :] - slots, 0), axis=2
    )
    targets = leaf_rows + shift * RB
    placed = jnp.zeros((group_rows, col_width), jnp.float32)
    placed = placed.at[targets.reshape(-1)].add(leaf_terms.reshape(-1, col_width))
    reduced = lax.psum_scatter(placed, "col", scatter_dimension=0, tiled=True)
    panels_win = gather_rows(prior_panels[:window_rows])
    partial = schur_block - jnp.dot(prior_panels, panels_win.T, precision=lax.Precision.HIGHEST)
    partial = lax.optimization_barrier(partial)
    updated = partial - reduced
    window_block = gather_rows_source_order(updated[:window_rows])
    return factor_solve(window_block, updated, lax.axis_size("row"), lax.axis_size("col"))


def solution(mesh):
    placed = (
        P(("row", "col"), None, None),
        P(("row", "col"), None, None),
        P(("row", "col"), None, None),
        P(("row", "col"), None),
        P(("row", "col")),
        P("row", None),
        P(("row", "col"), None),
        P(("row", "col"), None),
    )
    return jax.shard_map(
        body, mesh=mesh, in_specs=placed, out_specs=P(("row", "col"), None), check_vma=False
    )
```
